512 devices in a mesh: dom: 128 (over z, y, core), feat: 4 (over x).
Axes of the slice: x: 4, y: 8, z: 8, core: 2. Of those that a mesh axis runs over, the one named last changes fastest.
Arguments:
- features: bfloat16 [57344, 128], P('dom'), may hold values from -6 to 6
- perturb: bfloat16 [57344, 128], P('dom'), may hold values from -0.5 to 0.5
- w_self: bfloat16 [128, 1024], P(None, 'feat'), may hold values from -0.5 to 0.5
- w_neigh: bfloat16 [128, 1024], P(None, 'feat'), may hold values from -0.5 to 0.5
- bias: float32 [1024], P('feat'), may hold values from -3 to 3
- upstream: bfloat16 [57344, 1024], P('dom', 'feat'), may hold values from -0.0234375 to 0.0234375
- hub_rows: int32 [128, 2], P('dom'), may hold values from 0 to 447, as said below
- send_rows: int32 [128, 4, 56], P('dom'), may hold values from -1 to 447, as said below
- neighbors: int32 [57344, 15], P('dom'), may hold values from 0 to 927, as said below
Outputs:
- new_perturb: bfloat16 [57344, 128], P('dom', 'feat')
- grad_self: float32 [128, 1024], P(None, 'feat')
- grad_neigh: float32 [128, 1024], P(None, 'feat')
The draws below stay inside these ranges and needn't reach their ends.
Inputs may be any that keep to these rules, and one draw needn't show every extreme that they name: hub_rows[s] are distinct rows of partition s. send_rows[s, o] lists distinct rows of partition s sent to partition s + off(o) mod 128; live entries come first, at least 14 of them, and in every draw some list is full with 56 live entries. `neighbors`: indices below 448 are rows of the node's own partition; indices 448 + o * 56 + j refer only to live slots of the list that partition s = p - off(o) mod 128 sends to p; indices from 672 on are hub nodes.
All inputs are finite; a program needn't handle non-finite values.
Results may differ from the reference program's by a relative error of at most 0.001.
The reference program's roundings to bfloat16 on the way (of `perturbed`, `halo`, `hubs`, `table`, `neighbor_mean` and `grad_pre`) count: a program that leaves them out, or rounds other values in their place, can miss the bound.
Values may be sent and summed in bfloat16 or wider, within the bound.
No kernel may reach another device: no remote copies, remote signals or barrier semaphores. Data moves between devices by JAX's collectives and lax.ppermute only.
A program may use at most 64 MiB of HBM per device.

```python
import jax
import jax.numpy as jnp
from jax import lax

F_IN = 128
HIDDEN_SIZE = 1024
K = 15
R = 448
NOFF = 4
SLOT = 56
HUB_DEV = 2
DOMAINS = 128
NODES = 57344
HUBS = 256
TABLE = 928


def halo_counts(key):
    counts = jax.random.randint(jax.random.fold_in(key, 11), (DOMAINS * NOFF,), SLOT // 4, SLOT + 1)
    chosen = jax.random.randint(jax.random.fold_in(key, 12), (), 0, DOMAINS * NOFF)
    counts = jnp.where(jnp.arange(DOMAINS * NOFF) == chosen, SLOT, counts)
    return counts.reshape(DOMAINS, NOFF).astype(jnp.int32)


def draw_send_rows(key, part):
    counts = halo_counts(key)
    keys = jax.random.split(jax.random.fold_in(key, 13), DOMAINS * NOFF)
    shuffled = jax.vmap(lambda one: jax.random.permutation(one, R)[:SLOT])(keys)
    shuffled = shuffled.reshape(DOMAINS, NOFF, SLOT).astype(jnp.int32)
    slot_ids = jnp.arange(SLOT, dtype=jnp.int32)
    return jnp.where(slot_ids[None, None, :] < counts[:, :, None], shuffled, -1).astype(jnp.int32)


def draw_hub_rows(key, part):
    keys = jax.random.split(jax.random.fold_in(key, 14), DOMAINS)
    chosen = jax.vmap(lambda one: jax.random.permutation(one, R)[:HUB_DEV])(keys).astype(jnp.int32)
    top_part = jax.random.randint(jax.random.fold_in(key, 20), (), 0, DOMAINS)
    low_part = (top_part + 1) % DOMAINS
    top_list = chosen[top_part]
    top_list = jnp.where(top_list == R - 1, top_list[0], top_list).at[0].set(R - 1)
    low_list = chosen[low_part]
    low_list = jnp.where(low_list == 0, low_list[0], low_list).at[0].set(0)
    chosen = chosen.at[top_part].set(top_list)
    chosen = chosen.at[low_part].set(low_list)
    return chosen.astype(jnp.int32)


def draw_neighbors(key, part):
    counts = halo_counts(key)
    category = jax.random.randint(jax.random.fold_in(key, 15), (NODES, K), 0, 4)
    local_row = jax.random.randint(jax.random.fold_in(key, 16), (NODES, K), 0, R)
    direction = jax.random.randint(jax.random.fold_in(key, 17), (NODES, K), 0, NOFF)
    part_of = (jnp.arange(NODES, dtype=jnp.int32) // R)[:, None]
    offset = jnp.where(direction < 2, direction - 2, direction - 1)
    source_part = (part_of - offset) % DOMAINS
    live_count = counts[source_part, direction]
    slot_pick = jax.random.randint(jax.random.fold_in(key, 18), (NODES, K), 0, 2 ** 20) % live_count
    hub_pick = jax.random.randint(jax.random.fold_in(key, 19), (NODES, K), 0, HUBS)
    halo_index = R + direction * SLOT + slot_pick
    hub_index = R + NOFF * SLOT + hub_pick
    return jnp.where(category < 2, local_row, jnp.where(category == 2, halo_index, hub_index)).astype(jnp.int32)


def steps_of(key, extent, cuts, smallest, largest):
    def one(dim, parts):
        steps = jax.random.uniform(jax.random.fold_in(jax.random.fold_in(key, 6), dim), (parts,), jnp.float32, smallest / len(cuts), largest / len(cuts))
        return jnp.repeat(jnp.exp(steps), extent[dim] // parts).reshape((-1,) + (1,) * (len(extent) - dim - 1))

    loudness = one(*cuts[0])
    for cut in cuts[1:]:
        loudness = loudness * one(*cut)
    return loudness


def noise(own_key, extent, width, limit, cuts=(), kind=jnp.bfloat16):
    result = jax.random.normal(own_key, extent, jnp.float32) * width
    if len(cuts) > 0:
        result = steps_of(own_key, extent, cuts, -0.22, 0.18) * result
    return jnp.clip(result, min=-limit, max=limit).astype(kind)


def setup_inputs(seed: int = 0) -> dict:
    streams_of = jax.random.split(jax.random.key(seed), 10)
    features = noise(streams_of[0], (NODES, F_IN), 1.0, 6.0, ((0, 128),))
    perturb = jnp.clip(jax.random.uniform(streams_of[1], (NODES, F_IN), jnp.float32, -0.5, 0.5) * steps_of(streams_of[1], (NODES, F_IN), ((0, 128),), -0.4, 0.0), -0.5, 0.5).astype(jnp.bfloat16)
    w_self = noise(streams_of[2], (F_IN, HIDDEN_SIZE), F_IN ** -0.5, 0.5, ((1, 4),))
    w_neigh = noise(streams_of[3], (F_IN, HIDDEN_SIZE), F_IN ** -0.5, 0.5, ((1, 4),))
    bias = noise(streams_of[4], (HIDDEN_SIZE,), 0.5, 3.0, ((0, 4),), jnp.float32)
    upstream = noise(streams_of[5], (NODES, HIDDEN_SIZE), NODES ** -0.5, 0.0234375, ((0, 128), (1, 4)))
    hub_rows = draw_hub_rows(jax.random.fold_in(streams_of[9], 71), 0)
    send_rows = draw_send_rows(jax.random.fold_in(streams_of[9], 71), 0)
    neighbors = draw_neighbors(jax.random.fold_in(streams_of[9], 71), 0)
    return {"features": features, "perturb": perturb, "w_self": w_self, "w_neigh": w_neigh, "bias": bias, "upstream": upstream, "hub_rows": hub_rows, "send_rows": send_rows, "neighbors": neighbors}


def offset_of(direction):
    return direction - 2 if direction < 2 else direction - 1

def dense_part(blocks, w_self, w_neigh, bias):
    own_rows, mean_rows, cotangent = blocks
    preact = jnp.dot(own_rows, w_self, preferred_element_type=jnp.float32)
    preact = preact + jnp.dot(mean_rows, w_neigh, preferred_element_type=jnp.float32) + bias
    sigmoid_pre = jax.nn.sigmoid(preact)
    grad_pre = (cotangent.astype(jnp.float32) * sigmoid_pre * (1.0 + preact * (1.0 - sigmoid_pre))).astype(jnp.bfloat16)
    own_grad = jnp.dot(grad_pre, w_self.T, preferred_element_type=jnp.float32)
    spread = jnp.dot(grad_pre, w_neigh.T, preferred_element_type=jnp.float32) / K
    part_self = jnp.dot(own_rows.T, grad_pre, preferred_element_type=jnp.float32)
    part_neigh = jnp.dot(mean_rows.T, grad_pre, preferred_element_type=jnp.float32)
    return (own_grad, spread, part_self, part_neigh)

def reference(features, perturb, w_self, w_neigh, bias, upstream, hub_rows, send_rows, neighbors):
    perturbed = (features.astype(jnp.float32) + perturb.astype(jnp.float32)).astype(jnp.bfloat16)
    dom_ids = jnp.arange(DOMAINS, dtype=jnp.int32)
    halo_pieces = []
    for direction in range(NOFF):
        source_part = (dom_ids - offset_of(direction)) % DOMAINS
        row_list = send_rows[source_part, direction]
        flat_index = source_part[:, None] * R + jnp.maximum(row_list, 0)
        picked = perturbed[flat_index]
        halo_pieces.append(jnp.where((row_list >= 0)[:, :, None], picked, jnp.zeros((), jnp.bfloat16)))
    halo = jnp.concatenate(halo_pieces, axis=1)
    hub_index = (dom_ids[:, None] * R + hub_rows).reshape(-1)
    hubs = perturbed[hub_index]
    table = jnp.concatenate([perturbed.reshape(DOMAINS, R, F_IN), halo, jnp.broadcast_to(hubs[None], (DOMAINS, HUBS, F_IN))], axis=1)
    flat_table = table.reshape(DOMAINS * TABLE, F_IN)
    table_index = (jnp.arange(NODES, dtype=jnp.int32) // R * TABLE)[:, None] + neighbors
    gathered_sum = jnp.zeros((NODES, F_IN), jnp.float32)
    for position in range(K):
        gathered_sum = gathered_sum + flat_table[table_index[:, position]].astype(jnp.float32)
    neighbor_mean = (gathered_sum / K).astype(jnp.bfloat16)
    blocks = (perturbed.reshape(DOMAINS, R, F_IN), neighbor_mean.reshape(DOMAINS, R, F_IN), upstream.reshape(DOMAINS, R, HIDDEN_SIZE))
    own_grad, spread, part_self, part_neigh = lax.map(lambda blk: dense_part(blk, w_self, w_neigh, bias), blocks)
    grad_self = lax.optimization_barrier(jnp.sum(part_self, axis=0))
    grad_neigh = lax.optimization_barrier(jnp.sum(part_neigh, axis=0))
    own_grad = own_grad.reshape(NODES, F_IN)
    spread = spread.reshape(NODES, F_IN)
    table_grad = jnp.zeros((DOMAINS * TABLE, F_IN), jnp.float32)
    for position in range(K):
        table_grad = table_grad.at[table_index[:, position]].add(spread)
    table_grad = table_grad.reshape(DOMAINS, TABLE, F_IN)
    grad_in = own_grad + table_grad[:, :R].reshape(NODES, F_IN)
    for direction in range(NOFF):
        source_part = (dom_ids - offset_of(direction)) % DOMAINS
        row_list = send_rows[source_part, direction]
        target_index = jnp.where(row_list >= 0, source_part[:, None] * R + row_list, NODES)
        returned = table_grad[:, R + direction * SLOT:R + (direction + 1) * SLOT]
        grad_in = grad_in.at[target_index.reshape(-1)].add(returned.reshape(-1, F_IN), mode='drop')
    hub_total = lax.optimization_barrier(jnp.sum(table_grad[:, R + NOFF * SLOT:], axis=0))
    grad_in = grad_in.at[hub_index].add(hub_total)
    mean_square = lax.optimization_barrier(jnp.mean(grad_in * grad_in, axis=1, keepdims=True))
    new_perturb = (perturb.astype(jnp.float32) + 0.5 * grad_in / jnp.sqrt(mean_square + 1e-06)).astype(jnp.bfloat16)
    return (new_perturb, grad_self, grad_neigh)
```

```python
import jax
import jax.numpy as jnp
from jax import lax
from jax.sharding import PartitionSpec as P

K = 15
NOFF = 4
F32 = jnp.float32
BF16 = jnp.bfloat16
HIGH = lax.Precision.HIGHEST


def from_behind(x, axis, by):
    size = lax.axis_size(axis)
    return lax.ppermute(x, axis, [(i, (i + by) % size) for i in range(size)])


def offset_of(direction):
    return direction - 2 if direction < 2 else direction - 1


def contract_rows(left, right, precision=None):
    return lax.dot_general(
        left, right, (((0,), (0,)), ((), ())), preferred_element_type=F32, precision=precision
    )


def gather_all(x, axis):
    n = lax.axis_size(axis)
    rep = jnp.broadcast_to(x[None], (n,) + x.shape).reshape((n * x.shape[0],) + x.shape[1:])
    out = lax.all_to_all(rep, axis, 0, 0, tiled=True)
    return out.reshape((n,) + x.shape)


def per_device(features, perturb, w_self, w_neigh, bias, upstream, hub_rows, send_rows, neighbors):
    rows_here, feat_in = features.shape
    hidden_here = w_self.shape[1]
    slots = send_rows.shape[2]
    hub_dev = hub_rows.shape[1]
    dom_count = lax.axis_size("dom")
    feat_count = lax.axis_size("feat")
    column = lax.axis_index("feat")
    slice_width = feat_in // feat_count
    halo_rows = NOFF * slots
    table_rows = rows_here + halo_rows + dom_count * hub_dev

    perturbed = (features.astype(F32) + perturb.astype(F32)).astype(BF16)

    send_flat = send_rows[0].reshape(halo_rows)
    pick = (send_flat[:, None] == lax.broadcasted_iota(jnp.int32, (halo_rows, rows_here), 1))
    hub_pick = (hub_rows[0][:, None] == lax.broadcasted_iota(jnp.int32, (hub_dev, rows_here), 1))
    halo_out = jnp.dot(pick.astype(BF16), perturbed, preferred_element_type=F32).astype(BF16)
    hub_out = jnp.dot(hub_pick.astype(BF16), perturbed, preferred_element_type=F32).astype(BF16)

    pieces = [
        from_behind(halo_out[o * slots : (o + 1) * slots], "dom", offset_of(o)) for o in range(NOFF)
    ]
    hubs = gather_all(hub_out, "dom").reshape(dom_count * hub_dev, feat_in)
    table = jnp.concatenate([perturbed] + pieces + [hubs], 0)

    t_iota = lax.broadcasted_iota(jnp.int32, (rows_here, K, table_rows), 2)
    counts = jnp.sum((neighbors[:, :, None] == t_iota).astype(F32), axis=1)
    gathered_sum = jnp.dot(counts.astype(BF16), table, preferred_element_type=F32)
    neighbor_mean = (gathered_sum / K).astype(BF16)

    preact = jnp.dot(perturbed, w_self, preferred_element_type=F32)
    preact = preact + jnp.dot(neighbor_mean, w_neigh, preferred_element_type=F32) + bias
    sigmoid_pre = jax.nn.sigmoid(preact)
    grad_pre = (
        upstream.astype(F32) * sigmoid_pre * (1.0 + preact * (1.0 - sigmoid_pre))
    ).astype(BF16)
    part_self = contract_rows(perturbed, grad_pre)
    part_neigh = contract_rows(neighbor_mean, grad_pre)

    payload = jnp.concatenate([grad_pre, w_self, w_neigh], 0)
    got = gather_all(payload, "feat")
    gp_all = got[:, :rows_here]
    ws_all = got[:, rows_here : rows_here + feat_in]
    wn_all = got[:, rows_here + feat_in :]
    dims = (((0, 2), (0, 2)), ((), ()))
    own_grad = lax.dot_general(gp_all, ws_all, dims, preferred_element_type=F32)
    spread = lax.dot_general(gp_all, wn_all, dims, preferred_element_type=F32) / K

    table_grad = contract_rows(counts, spread, HIGH)

    returned = jnp.concatenate(
        [
            from_behind(
                table_grad[rows_here + o * slots : rows_here + (o + 1) * slots],
                "dom",
                -offset_of(o),
            )
            for o in range(NOFF)
        ],
        0,
    )

    weight_flat = jnp.concatenate([part_self.reshape(-1), part_neigh.reshape(-1)])
    weight_chunks = weight_flat.reshape(dom_count, -1)
    hub_chunks = table_grad[rows_here + halo_rows :].reshape(dom_count, hub_dev * feat_in)
    sent = jnp.concatenate([hub_chunks, weight_chunks], 1)
    recv = lax.all_to_all(sent, "dom", 0, 0, tiled=True)
    totals = jnp.sum(recv, axis=0)
    hub_total = totals[: hub_dev * feat_in].reshape(hub_dev, feat_in)
    weight_part = totals[hub_dev * feat_in :]

    grad_in = own_grad + table_grad[:rows_here]
    grad_in = grad_in + contract_rows(pick.astype(F32), returned, HIGH)
    grad_in = grad_in + contract_rows(hub_pick.astype(F32), hub_total, HIGH)

    mean_square = jnp.mean(grad_in * grad_in, axis=1, keepdims=True)
    own_cols = lax.dynamic_slice_in_dim(grad_in, column * slice_width, slice_width, 1)
    own_perturb = lax.dynamic_slice_in_dim(perturb, column * slice_width, slice_width, 1).astype(F32)
    new_perturb = (own_perturb + 0.5 * own_cols / jnp.sqrt(mean_square + 1e-06)).astype(BF16)

    weights = gather_all(weight_part, "dom").reshape(2, feat_in, hidden_here)
    return (new_perturb, weights[0], weights[1])


def solution(mesh):
    in_specs = (
        P("dom", None),
        P("dom", None),
        P(None, "feat"),
        P(None, "feat"),
        P("feat"),
        P("dom", "feat"),
        P("dom", None),
        P("dom", None, None),
        P("dom", None),
    )
    out_specs = (P("dom", "feat"), P(None, "feat"), P(None, "feat"))
    return jax.shard_map(
        per_device, mesh=mesh, in_specs=in_specs, out_specs=out_specs, check_vma=False
    )
```

```python
import jax
import jax.numpy as jnp
from jax import lax
from jax.sharding import PartitionSpec as P

K = 15
NOFF = 4
F32 = jnp.float32
BF16 = jnp.bfloat16
HIGH = lax.Precision.HIGHEST


def from_behind(x, axis, by):
    size = lax.axis_size(axis)
    return lax.ppermute(x, axis, [(i, (i + by) % size) for i in range(size)])


def offset_of(direction):
    return direction - 2 if direction < 2 else direction - 1


def contract_rows(left, right, precision=None):
    return lax.dot_general(
        left, right, (((0,), (0,)), ((), ())), preferred_element_type=F32, precision=precision
    )


def gather_all(x, axis):
    n = lax.axis_size(axis)
    rep = jnp.broadcast_to(x[None], (n,) + x.shape).reshape((n * x.shape[0],) + x.shape[1:])
    out = lax.all_to_all(rep, axis, 0, 0, tiled=True)
    return out.reshape((n,) + x.shape)


def per_device(features, perturb, w_self, w_neigh, bias, upstream, hub_rows, send_rows, neighbors):
    rows_here, feat_in = features.shape
    hidden_here = w_self.shape[1]
    slots = send_rows.shape[2]
    hub_dev = hub_rows.shape[1]
    dom_count = lax.axis_size("dom")
    feat_count = lax.axis_size("feat")
    column = lax.axis_index("feat")
    slice_width = feat_in // feat_count
    halo_rows = NOFF * slots
    table_rows = rows_here + halo_rows + dom_count * hub_dev

    bias_hi = lax.reduce_precision(bias, exponent_bits=8, mantissa_bits=7)
    bias_rest = bias - bias_hi
    bias_mid = lax.reduce_precision(bias_rest, exponent_bits=8, mantissa_bits=7)
    bias_lo = bias_rest - bias_mid
    bias_parts = jnp.stack([bias_hi, bias_mid, bias_lo]).astype(BF16)
    payload = jnp.concatenate([upstream, w_self, w_neigh, bias_parts], 0)
    got = gather_all(payload, "feat")
    up_all = got[:, :rows_here]
    ws_all = got[:, rows_here : rows_here + feat_in]
    wn_all = got[:, rows_here + feat_in : rows_here + 2 * feat_in]
    bias_all = jnp.sum(got[:, rows_here + 2 * feat_in :].astype(F32), axis=1)

    perturbed = (features.astype(F32) + perturb.astype(F32)).astype(BF16)

    send_flat = send_rows[0].reshape(halo_rows)
    pick = (send_flat[:, None] == lax.broadcasted_iota(jnp.int32, (halo_rows, rows_here), 1))
    hub_pick = (hub_rows[0][:, None] == lax.broadcasted_iota(jnp.int32, (hub_dev, rows_here), 1))
    halo_out = jnp.dot(pick.astype(BF16), perturbed, preferred_element_type=F32).astype(BF16)
    hub_out = jnp.dot(hub_pick.astype(BF16), perturbed, preferred_element_type=F32).astype(BF16)

    pieces = [
        from_behind(halo_out[o * slots : (o + 1) * slots], "dom", offset_of(o)) for o in range(NOFF)
    ]
    hubs = gather_all(hub_out, "dom").reshape(dom_count * hub_dev, feat_in)
    table = jnp.concatenate([perturbed] + pieces + [hubs], 0)

    t_iota = lax.broadcasted_iota(jnp.int32, (rows_here, K, table_rows), 2)
    counts = jnp.sum((neighbors[:, :, None] == t_iota).astype(F32), axis=1)
    gathered_sum = jnp.dot(counts.astype(BF16), table, preferred_element_type=F32)
    neighbor_mean = (gathered_sum / K).astype(BF16)

    preact = jnp.einsum("nc,fch->fnh", perturbed, ws_all, preferred_element_type=F32)
    preact = preact + jnp.einsum("nc,fch->fnh", neighbor_mean, wn_all, preferred_element_type=F32)
    preact = preact + bias_all[:, None, :]
    sigmoid_pre = jax.nn.sigmoid(preact)
    gp_all = (
        up_all.astype(F32) * sigmoid_pre * (1.0 + preact * (1.0 - sigmoid_pre))
    ).astype(BF16)
    grad_pre = lax.dynamic_index_in_dim(gp_all, column, 0, keepdims=False)
    part_self = contract_rows(perturbed, grad_pre)
    part_neigh = contract_rows(neighbor_mean, grad_pre)

    weight_flat = jnp.concatenate([part_self.reshape(-1), part_neigh.reshape(-1)])
    weight_recv = lax.all_to_all(weight_flat.reshape(dom_count, -1), "dom", 0, 0, tiled=True)

    dims = (((0, 2), (0, 2)), ((), ()))
    own_grad = lax.dot_general(gp_all, ws_all, dims, preferred_element_type=F32)
    spread = lax.dot_general(gp_all, wn_all, dims, preferred_element_type=F32) / K

    table_grad = contract_rows(counts, spread, HIGH)

    returned = jnp.concatenate(
        [
            from_behind(
                table_grad[rows_here + o * slots : rows_here + (o + 1) * slots],
                "dom",
                -offset_of(o),
            )
            for o in range(NOFF)
        ],
        0,
    )

    weight_part = jnp.sum(weight_recv, axis=0)
    hub_chunks = table_grad[rows_here + halo_rows :].reshape(dom_count, hub_dev * feat_in)
    weight_rep = jnp.broadcast_to(weight_part[None], (dom_count, weight_part.shape[0]))
    sent = jnp.concatenate([hub_chunks, weight_rep], 1)
    recv = lax.all_to_all(sent, "dom", 0, 0, tiled=True)
    hub_total = jnp.sum(recv[:, : hub_dev * feat_in], axis=0).reshape(hub_dev, feat_in)
    weights = recv[:, hub_dev * feat_in :].reshape(2, feat_in, hidden_here)

    grad_in = own_grad + table_grad[:rows_here]
    grad_in = grad_in + contract_rows(pick.astype(F32), returned, HIGH)
    grad_in = grad_in + contract_rows(hub_pick.astype(F32), hub_total, HIGH)

    mean_square = jnp.mean(grad_in * grad_in, axis=1, keepdims=True)
    own_cols = lax.dynamic_slice_in_dim(grad_in, column * slice_width, slice_width, 1)
    own_perturb = lax.dynamic_slice_in_dim(perturb, column * slice_width, slice_width, 1).astype(F32)
    new_perturb = (own_perturb + 0.5 * own_cols / jnp.sqrt(mean_square + 1e-06)).astype(BF16)

    return (new_perturb, weights[0], weights[1])


def solution(mesh):
    in_specs = (
        P("dom", None),
        P("dom", None),
        P(None, "feat"),
        P(None, "feat"),
        P("feat"),
        P("dom", "feat"),
        P("dom", None),
        P("dom", None, None),
        P("dom", None),
    )
    out_specs = (P("dom", "feat"), P(None, "feat"), P(None, "feat"))
    return jax.shard_map(
        per_device, mesh=mesh, in_specs=in_specs, out_specs=out_specs, check_vma=False
    )
```

```python
import jax
import jax.numpy as jnp
from jax import lax
from jax.sharding import PartitionSpec as P

K = 15
NOFF = 4
F32 = jnp.float32
BF16 = jnp.bfloat16
HIGH = lax.Precision.HIGHEST


def from_behind(x, axis, by):
    size = lax.axis_size(axis)
    return lax.ppermute(x, axis, [(i, (i + by) % size) for i in range(size)])


def offset_of(direction):
    return direction - 2 if direction < 2 else direction - 1


def contract_rows(left, right, precision=None):
    return lax.dot_general(
        left, right, (((0,), (0,)), ((), ())), preferred_element_type=F32, precision=precision
    )


def gather_all(x, axis):
    n = lax.axis_size(axis)
    rep = jnp.broadcast_to(x[None], (n,) + x.shape).reshape((n * x.shape[0],) + x.shape[1:])
    out = lax.all_to_all(rep, axis, 0, 0, tiled=True)
    return out.reshape((n,) + x.shape)


def per_device(features, perturb, w_self, w_neigh, bias, upstream, hub_rows, send_rows, neighbors):
    rows_here, feat_in = features.shape
    hidden_here = w_self.shape[1]
    slots = send_rows.shape[2]
    hub_dev = hub_rows.shape[1]
    dom_count = lax.axis_size("dom")
    feat_count = lax.axis_size("feat")
    column = lax.axis_index("feat")
    slice_width = feat_in // feat_count
    halo_rows = NOFF * slots
    table_rows = rows_here + halo_rows + dom_count * hub_dev

    bias_hi = lax.reduce_precision(bias, exponent_bits=8, mantissa_bits=7)
    bias_rest = bias - bias_hi
    bias_mid = lax.reduce_precision(bias_rest, exponent_bits=8, mantissa_bits=7)
    bias_lo = bias_rest - bias_mid
    bias_parts = jnp.stack([bias_hi, bias_mid, bias_lo]).astype(BF16)
    payload = jnp.concatenate([upstream, w_self, w_neigh, bias_parts], 0)
    got = jnp.stack(
        [payload] + [from_behind(payload, "feat", shift) for shift in range(1, feat_count)]
    )
    up_all = got[:, :rows_here]
    ws_all = got[:, rows_here : rows_here + feat_in]
    wn_all = got[:, rows_here + feat_in : rows_here + 2 * feat_in]
    bias_all = jnp.sum(got[:, rows_here + 2 * feat_in :].astype(F32), axis=1)

    perturbed = (features.astype(F32) + perturb.astype(F32)).astype(BF16)

    send_flat = send_rows[0].reshape(halo_rows)
    pick = (send_flat[:, None] == lax.broadcasted_iota(jnp.int32, (halo_rows, rows_here), 1))
    hub_pick = (hub_rows[0][:, None] == lax.broadcasted_iota(jnp.int32, (hub_dev, rows_here), 1))
    halo_out = jnp.dot(pick.astype(BF16), perturbed, preferred_element_type=F32).astype(BF16)
    hub_out = jnp.dot(hub_pick.astype(BF16), perturbed, preferred_element_type=F32).astype(BF16)

    pieces = [
        from_behind(halo_out[o * slots : (o + 1) * slots], "dom", offset_of(o)) for o in range(NOFF)
    ]
    hubs = gather_all(hub_out, "dom").reshape(dom_count * hub_dev, feat_in)
    table = jnp.concatenate([perturbed] + pieces + [hubs], 0)

    t_iota = lax.broadcasted_iota(jnp.int32, (rows_here, K, table_rows), 2)
    counts = jnp.sum((neighbors[:, :, None] == t_iota).astype(F32), axis=1)
    gathered_sum = jnp.dot(counts.astype(BF16), table, preferred_element_type=F32)
    neighbor_mean = (gathered_sum / K).astype(BF16)

    preact = jnp.einsum("nc,fch->fnh", perturbed, ws_all, preferred_element_type=F32)
    preact = preact + jnp.einsum("nc,fch->fnh", neighbor_mean, wn_all, preferred_element_type=F32)
    preact = preact + bias_all[:, None, :]
    sigmoid_pre = jax.nn.sigmoid(preact)
    gp_all = (
        up_all.astype(F32) * sigmoid_pre * (1.0 + preact * (1.0 - sigmoid_pre))
    ).astype(BF16)
    grad_pre = gp_all[0]
    part_self = contract_rows(perturbed, grad_pre)
    part_neigh = contract_rows(neighbor_mean, grad_pre)

    weight_flat = jnp.concatenate([part_self.reshape(-1), part_neigh.reshape(-1)])
    weight_recv = lax.all_to_all(weight_flat.reshape(dom_count, -1), "dom", 0, 0, tiled=True)

    dims = (((0, 2), (0, 2)), ((), ()))
    own_grad = lax.dot_general(gp_all, ws_all, dims, preferred_element_type=F32)
    spread = lax.dot_general(gp_all, wn_all, dims, preferred_element_type=F32) / K

    table_grad = contract_rows(counts, spread, HIGH)

    returned = jnp.concatenate(
        [
            from_behind(
                table_grad[rows_here + o * slots : rows_here + (o + 1) * slots],
                "dom",
                -offset_of(o),
            )
            for o in range(NOFF)
        ],
        0,
    )

    weight_part = jnp.sum(weight_recv, axis=0)
    hub_chunks = table_grad[rows_here + halo_rows :].reshape(dom_count, hub_dev * feat_in)
    weight_rep = jnp.broadcast_to(weight_part[None], (dom_count, weight_part.shape[0]))
    sent = jnp.concatenate([hub_chunks, weight_rep], 1)
    recv = lax.all_to_all(sent, "dom", 0, 0, tiled=True)
    hub_total = jnp.sum(recv[:, : hub_dev * feat_in], axis=0).reshape(hub_dev, feat_in)
    weights = recv[:, hub_dev * feat_in :].reshape(2, feat_in, hidden_here)

    grad_in = own_grad + table_grad[:rows_here]
    grad_in = grad_in + contract_rows(pick.astype(F32), returned, HIGH)
    grad_in = grad_in + contract_rows(hub_pick.astype(F32), hub_total, HIGH)

    mean_square = jnp.mean(grad_in * grad_in, axis=1, keepdims=True)
    own_cols = lax.dynamic_slice_in_dim(grad_in, column * slice_width, slice_width, 1)
    own_perturb = lax.dynamic_slice_in_dim(perturb, column * slice_width, slice_width, 1).astype(F32)
    new_perturb = (own_perturb + 0.5 * own_cols / jnp.sqrt(mean_square + 1e-06)).astype(BF16)

    return (new_perturb, weights[0], weights[1])


def solution(mesh):
    in_specs = (
        P("dom", None),
        P("dom", None),
        P(None, "feat"),
        P(None, "feat"),
        P("feat"),
        P("dom", "feat"),
        P("dom", None),
        P("dom", None, None),
        P("dom", None),
    )
    out_specs = (P("dom", "feat"), P(None, "feat"), P(None, "feat"))
    return jax.shard_map(
        per_device, mesh=mesh, in_specs=in_specs, out_specs=out_specs, check_vma=False
    )
```

```python
import jax
import jax.numpy as jnp
from jax import lax
from jax.sharding import PartitionSpec as P

K = 15
NOFF = 4
F32 = jnp.float32
BF16 = jnp.bfloat16
HIGH = lax.Precision.HIGHEST


def from_behind(x, axis, by):
    size = lax.axis_size(axis)
    return lax.ppermute(x, axis, [(i, (i + by) % size) for i in range(size)])


def offset_of(direction):
    return direction - 2 if direction < 2 else direction - 1


def contract_rows(left, right, precision=None):
    return lax.dot_general(
        left, right, (((0,), (0,)), ((), ())), preferred_element_type=F32, precision=precision
    )


def gather_all(x, axis):
    n = lax.axis_size(axis)
    rep = jnp.broadcast_to(x[None], (n,) + x.shape).reshape((n * x.shape[0],) + x.shape[1:])
    out = lax.all_to_all(rep, axis, 0, 0, tiled=True)
    return out.reshape((n,) + x.shape)


def per_device(features, perturb, w_self, w_neigh, bias, upstream, hub_rows, send_rows, neighbors):
    rows_here, feat_in = features.shape
    hidden_here = w_self.shape[1]
    slots = send_rows.shape[2]
    hub_dev = hub_rows.shape[1]
    dom_count = lax.axis_size("dom")
    feat_count = lax.axis_size("feat")
    column = lax.axis_index("feat")
    slice_width = feat_in // feat_count
    halo_rows = NOFF * slots
    table_rows = rows_here + halo_rows + dom_count * hub_dev

    bias_hi = lax.reduce_precision(bias, exponent_bits=8, mantissa_bits=7)
    bias_rest = bias - bias_hi
    bias_mid = lax.reduce_precision(bias_rest, exponent_bits=8, mantissa_bits=7)
    bias_lo = bias_rest - bias_mid
    bias_parts = jnp.stack([bias_hi, bias_mid, bias_lo]).astype(BF16)
    payload = jnp.concatenate([upstream, w_self, w_neigh, bias_parts], 0)
    got = jnp.stack(
        [payload] + [from_behind(payload, "feat", shift) for shift in range(1, feat_count)]
    )
    up_all = got[:, :rows_here]
    ws_all = got[:, rows_here : rows_here + feat_in]
    wn_all = got[:, rows_here + feat_in : rows_here + 2 * feat_in]
    bias_all = jnp.sum(got[:, rows_here + 2 * feat_in :].astype(F32), axis=1)

    perturbed = (features.astype(F32) + perturb.astype(F32)).astype(BF16)

    send_flat = send_rows[0].reshape(halo_rows)
    pick = (send_flat[:, None] == lax.broadcasted_iota(jnp.int32, (halo_rows, rows_here), 1))
    hub_pick = (hub_rows[0][:, None] == lax.broadcasted_iota(jnp.int32, (hub_dev, rows_here), 1))
    halo_out = jnp.dot(pick.astype(BF16), perturbed, preferred_element_type=F32).astype(BF16)
    hub_out = jnp.dot(hub_pick.astype(BF16), perturbed, preferred_element_type=F32).astype(BF16)

    pieces = [
        from_behind(halo_out[o * slots : (o + 1) * slots], "dom", offset_of(o)) for o in range(NOFF)
    ]
    hubs = gather_all(hub_out, "dom").reshape(dom_count * hub_dev, feat_in)
    table = jnp.concatenate([perturbed] + pieces + [hubs], 0)

    t_iota = lax.broadcasted_iota(jnp.int32, (rows_here, K, table_rows), 2)
    counts = jnp.sum((neighbors[:, :, None] == t_iota).astype(F32), axis=1)
    gathered_sum = jnp.dot(counts.astype(BF16), table, preferred_element_type=F32)
    neighbor_mean = (gathered_sum / K).astype(BF16)

    preact = jnp.einsum("nc,fch->fnh", perturbed, ws_all, preferred_element_type=F32)
    preact = preact + jnp.einsum("nc,fch->fnh", neighbor_mean, wn_all, preferred_element_type=F32)
    preact = preact + bias_all[:, None, :]
    sigmoid_pre = jax.nn.sigmoid(preact)
    gp_all = (
        up_all.astype(F32) * sigmoid_pre * (1.0 + preact * (1.0 - sigmoid_pre))
    ).astype(BF16)
    grad_pre = gp_all[0]
    part_self = contract_rows(perturbed, grad_pre)
    part_neigh = contract_rows(neighbor_mean, grad_pre)

    weight_flat = jnp.concatenate([part_self.reshape(-1), part_neigh.reshape(-1)])
    weight_recv = lax.all_to_all(weight_flat.reshape(dom_count, -1), "dom", 0, 0, tiled=True)

    dims = (((0, 2), (0, 2)), ((), ()))
    own_grad = lax.dot_general(gp_all, ws_all, dims, preferred_element_type=F32)
    spread = lax.dot_general(gp_all, wn_all, dims, preferred_element_type=F32) / K

    table_grad = contract_rows(counts, spread, HIGH)

    returned = jnp.concatenate(
        [
            from_behind(
                table_grad[rows_here + o * slots : rows_here + (o + 1) * slots],
                "dom",
                -offset_of(o),
            )
            for o in range(NOFF)
        ],
        0,
    )

    weight_part = jnp.sum(weight_recv, axis=0)
    hub_chunks = table_grad[rows_here + halo_rows :].reshape(dom_count, hub_dev * feat_in)
    hub_chunks, returned = lax.optimization_barrier((hub_chunks, returned))
    weight_rep = jnp.broadcast_to(weight_part[None], (dom_count, weight_part.shape[0]))
    sent = jnp.concatenate([hub_chunks, weight_rep], 1)
    recv = lax.all_to_all(sent, "dom", 0, 0, tiled=True)
    hub_total = jnp.sum(recv[:, : hub_dev * feat_in], axis=0).reshape(hub_dev, feat_in)
    weights = recv[:, hub_dev * feat_in :].reshape(2, feat_in, hidden_here)

    grad_in = own_grad + table_grad[:rows_here]
    grad_in = grad_in + contract_rows(pick.astype(F32), returned, HIGH)
    grad_in = grad_in + contract_rows(hub_pick.astype(F32), hub_total, HIGH)

    mean_square = jnp.mean(grad_in * grad_in, axis=1, keepdims=True)
    own_cols = lax.dynamic_slice_in_dim(grad_in, column * slice_width, slice_width, 1)
    own_perturb = lax.dynamic_slice_in_dim(perturb, column * slice_width, slice_width, 1).astype(F32)
    new_perturb = (own_perturb + 0.5 * own_cols / jnp.sqrt(mean_square + 1e-06)).astype(BF16)

    return (new_perturb, weights[0], weights[1])


def solution(mesh):
    in_specs = (
        P("dom", None),
        P("dom", None),
        P(None, "feat"),
        P(None, "feat"),
        P("feat"),
        P("dom", "feat"),
        P("dom", None),
        P("dom", None, None),
        P("dom", None),
    )
    out_specs = (P("dom", "feat"), P(None, "feat"), P(None, "feat"))
    return jax.shard_map(
        per_device, mesh=mesh, in_specs=in_specs, out_specs=out_specs, check_vma=False
    )
```

```python
import jax
import jax.numpy as jnp
from jax import lax
from jax.sharding import PartitionSpec as P


K = 15
NOFF = 4
F32 = jnp.float32
BF16 = jnp.bfloat16
HIGH = lax.Precision.HIGHEST


def from_behind(x, axis, by):
    size = lax.axis_size(axis)
    return lax.ppermute(x, axis, [(i, (i + by) % size) for i in range(size)])


def offset_of(direction):
    return direction - 2 if direction < 2 else direction - 1


def contract_rows(left, right, precision=None):
    return lax.dot_general(
        left, right, (((0,), (0,)), ((), ())), preferred_element_type=F32, precision=precision
    )


def gather_all(x, axis):
    n = lax.axis_size(axis)
    rep = jnp.broadcast_to(x[None], (n,) + x.shape).reshape((n * x.shape[0],) + x.shape[1:])
    out = lax.all_to_all(rep, axis, 0, 0, tiled=True)
    return out.reshape((n,) + x.shape)


def per_device(features, perturb, w_self, w_neigh, bias, upstream, hub_rows, send_rows, neighbors):
    rows_here, feat_in = features.shape
    hidden_here = w_self.shape[1]
    slots = send_rows.shape[2]
    hub_dev = hub_rows.shape[1]
    dom_count = lax.axis_size("dom")
    feat_count = lax.axis_size("feat")
    column = lax.axis_index("feat")
    slice_width = feat_in // feat_count
    halo_rows = NOFF * slots
    table_rows = rows_here + halo_rows + dom_count * hub_dev

    perturbed = (features.astype(F32) + perturb.astype(F32)).astype(BF16)

    send_flat = send_rows[0].reshape(halo_rows)
    pick = (send_flat[:, None] == lax.broadcasted_iota(jnp.int32, (halo_rows, rows_here), 1))
    hub_pick = (hub_rows[0][:, None] == lax.broadcasted_iota(jnp.int32, (hub_dev, rows_here), 1))
    halo_out = jnp.dot(pick.astype(BF16), perturbed, preferred_element_type=F32).astype(BF16)
    hub_out = jnp.dot(hub_pick.astype(BF16), perturbed, preferred_element_type=F32).astype(BF16)

    pieces = [
        from_behind(halo_out[o * slots : (o + 1) * slots], "dom", offset_of(o))
        for o in range(NOFF)
    ]
    t_iota = lax.broadcasted_iota(jnp.int32, (rows_here, K, table_rows), 2)
    counts = jnp.sum((neighbors[:, :, None] == t_iota).astype(F32), axis=1)
    hub_out, counts = lax.optimization_barrier((hub_out, counts))

    hubs = gather_all(hub_out, "dom").reshape(dom_count * hub_dev, feat_in)
    table = jnp.concatenate([perturbed] + pieces + [hubs], 0)
    gathered_sum = jnp.dot(counts.astype(BF16), table, preferred_element_type=F32)
    neighbor_mean = (gathered_sum / K).astype(BF16)

    preact = jnp.dot(perturbed, w_self, preferred_element_type=F32)
    preact = preact + jnp.dot(neighbor_mean, w_neigh, preferred_element_type=F32) + bias
    sigmoid_pre = jax.nn.sigmoid(preact)
    grad_pre = (
        upstream.astype(F32) * sigmoid_pre * (1.0 + preact * (1.0 - sigmoid_pre))
    ).astype(BF16)

    payload = jnp.concatenate([grad_pre, w_self, w_neigh], 0)
    got = jnp.stack(
        [payload] + [from_behind(payload, "feat", shift) for shift in range(1, feat_count)]
    )

    part_self = contract_rows(perturbed, grad_pre)
    part_neigh = contract_rows(neighbor_mean, grad_pre)
    weight_flat = jnp.concatenate([part_self.reshape(-1), part_neigh.reshape(-1)])
    weight_recv = lax.all_to_all(weight_flat.reshape(dom_count, -1), "dom", 0, 0, tiled=True)

    gp_all = got[:, :rows_here]
    ws_all = got[:, rows_here : rows_here + feat_in]
    wn_all = got[:, rows_here + feat_in :]
    dims = (((0, 2), (0, 2)), ((), ()))
    own_grad = lax.dot_general(gp_all, ws_all, dims, preferred_element_type=F32)
    spread = lax.dot_general(gp_all, wn_all, dims, preferred_element_type=F32) / K

    table_grad = contract_rows(counts, spread, HIGH)

    returned = jnp.concatenate(
        [
            from_behind(
                table_grad[rows_here + o * slots : rows_here + (o + 1) * slots],
                "dom",
                -offset_of(o),
            )
            for o in range(NOFF)
        ],
        0,
    )

    weight_part = jnp.sum(weight_recv, axis=0)
    hub_chunks = table_grad[rows_here + halo_rows :].reshape(dom_count, hub_dev * feat_in)
    weight_rep = jnp.broadcast_to(weight_part[None], (dom_count, weight_part.shape[0]))
    sent = jnp.concatenate([hub_chunks, weight_rep], 1)
    recv = lax.all_to_all(sent, "dom", 0, 0, tiled=True)
    hub_total = jnp.sum(recv[:, : hub_dev * feat_in], axis=0).reshape(hub_dev, feat_in)
    weights = recv[:, hub_dev * feat_in :].reshape(2, feat_in, hidden_here)

    grad_in = own_grad + table_grad[:rows_here]
    grad_in = grad_in + contract_rows(pick.astype(F32), returned, HIGH)
    grad_in = grad_in + contract_rows(hub_pick.astype(F32), hub_total, HIGH)

    mean_square = jnp.mean(grad_in * grad_in, axis=1, keepdims=True)
    own_cols = lax.dynamic_slice_in_dim(grad_in, column * slice_width, slice_width, 1)
    own_perturb = lax.dynamic_slice_in_dim(perturb, column * slice_width, slice_width, 1).astype(F32)
    new_perturb = (own_perturb + 0.5 * own_cols / jnp.sqrt(mean_square + 1e-06)).astype(BF16)

    return (new_perturb, weights[0], weights[1])


def solution(mesh):
    in_specs = (
        P("dom", None),
        P("dom", None),
        P(None, "feat"),
        P(None, "feat"),
        P("feat"),
        P("dom", "feat"),
        P("dom", None),
        P("dom", None, None),
        P("dom", None),
    )
    out_specs = (P("dom", "feat"), P(None, "feat"), P(None, "feat"))

    return jax.shard_map(per_device, mesh=mesh, in_specs=in_specs, out_specs=out_specs, check_vma=False)
```

```python
import jax
import jax.numpy as jnp
from jax import lax
from jax.sharding import PartitionSpec as P


K = 15
NOFF = 4
F32 = jnp.float32
BF16 = jnp.bfloat16
HIGH = lax.Precision.HIGHEST


def from_behind(x, axis, by):
    size = lax.axis_size(axis)
    return lax.ppermute(x, axis, [(i, (i + by) % size) for i in range(size)])


def offset_of(direction):
    return direction - 2 if direction < 2 else direction - 1


def contract_rows(left, right, precision=None):
    return lax.dot_general(
        left, right, (((0,), (0,)), ((), ())), preferred_element_type=F32, precision=precision
    )


def gather_all(x, axis):
    n = lax.axis_size(axis)
    rep = jnp.broadcast_to(x[None], (n,) + x.shape).reshape((n * x.shape[0],) + x.shape[1:])
    out = lax.all_to_all(rep, axis, 0, 0, tiled=True)
    return out.reshape((n,) + x.shape)


def per_device(features, perturb, w_self, w_neigh, bias, upstream, hub_rows, send_rows, neighbors):
    rows_here, feat_in = features.shape
    hidden_here = w_self.shape[1]
    slots = send_rows.shape[2]
    hub_dev = hub_rows.shape[1]
    dom_count = lax.axis_size("dom")
    feat_count = lax.axis_size("feat")
    column = lax.axis_index("feat")
    slice_width = feat_in // feat_count
    halo_rows = NOFF * slots
    table_rows = rows_here + halo_rows + dom_count * hub_dev

    perturbed = (features.astype(F32) + perturb.astype(F32)).astype(BF16)

    send_flat = send_rows[0].reshape(halo_rows)
    pick = (send_flat[:, None] == lax.broadcasted_iota(jnp.int32, (halo_rows, rows_here), 1))
    hub_pick = (hub_rows[0][:, None] == lax.broadcasted_iota(jnp.int32, (hub_dev, rows_here), 1))
    halo_out = jnp.dot(pick.astype(BF16), perturbed, preferred_element_type=F32).astype(BF16)
    hub_out = jnp.dot(hub_pick.astype(BF16), perturbed, preferred_element_type=F32).astype(BF16)

    pieces = [
        from_behind(halo_out[o * slots : (o + 1) * slots], "dom", offset_of(o))
        for o in range(NOFF)
    ]
    t_iota = lax.broadcasted_iota(jnp.int32, (rows_here, K, table_rows), 2)
    counts = jnp.sum((neighbors[:, :, None] == t_iota).astype(F32), axis=1)
    hub_out, counts = lax.optimization_barrier((hub_out, counts))

    hubs = gather_all(hub_out, "dom").reshape(dom_count * hub_dev, feat_in)
    table = jnp.concatenate([perturbed] + pieces + [hubs], 0)
    gathered_sum = jnp.dot(counts.astype(BF16), table, preferred_element_type=F32)
    neighbor_mean = (gathered_sum / K).astype(BF16)

    preact = jnp.dot(perturbed, w_self, preferred_element_type=F32)
    preact = preact + jnp.dot(neighbor_mean, w_neigh, preferred_element_type=F32) + bias
    sigmoid_pre = jax.nn.sigmoid(preact)
    grad_pre = (
        upstream.astype(F32) * sigmoid_pre * (1.0 + preact * (1.0 - sigmoid_pre))
    ).astype(BF16)

    payload = jnp.concatenate([grad_pre, w_self, w_neigh], 0)
    got = jnp.stack(
        [payload] + [from_behind(payload, "feat", shift) for shift in range(1, feat_count)]
    )

    part_self = contract_rows(perturbed, grad_pre)
    part_neigh = contract_rows(neighbor_mean, grad_pre)
    weight_flat = jnp.concatenate([part_self.reshape(-1), part_neigh.reshape(-1)])
    weight_recv = lax.all_to_all(weight_flat.reshape(dom_count, -1), "dom", 0, 0, tiled=True)

    gp_all = got[:, :rows_here]
    ws_all = got[:, rows_here : rows_here + feat_in]
    wn_all = got[:, rows_here + feat_in :]
    dims = (((0, 2), (0, 2)), ((), ()))
    own_grad = lax.dot_general(gp_all, ws_all, dims, preferred_element_type=F32)
    spread = lax.dot_general(gp_all, wn_all, dims, preferred_element_type=F32) / K

    table_grad = contract_rows(counts, spread, HIGH)

    back = []
    for o in range(NOFF):
        back.append(
            from_behind(
                table_grad[rows_here + o * slots : rows_here + (o + 1) * slots],
                "dom",
                -offset_of(o),
            )
        )
    returned = jnp.concatenate(back, 0)

    weight_part = jnp.sum(weight_recv, axis=0)
    hub_chunks = table_grad[rows_here + halo_rows :].reshape(dom_count, hub_dev * feat_in)
    weight_rep = jnp.broadcast_to(weight_part[None], (dom_count, weight_part.shape[0]))
    sent = jnp.concatenate([hub_chunks, weight_rep], 1)
    recv = lax.all_to_all(sent, "dom", 0, 0, tiled=True)
    hub_total = jnp.sum(recv[:, : hub_dev * feat_in], axis=0).reshape(hub_dev, feat_in)
    weights = recv[:, hub_dev * feat_in :].reshape(2, feat_in, hidden_here)

    grad_in = own_grad + table_grad[:rows_here]
    grad_in = grad_in + contract_rows(pick.astype(F32), returned, HIGH)
    grad_in = grad_in + contract_rows(hub_pick.astype(F32), hub_total, HIGH)

    mean_square = jnp.mean(grad_in * grad_in, axis=1, keepdims=True)
    own_cols = lax.dynamic_slice_in_dim(grad_in, column * slice_width, slice_width, 1)
    own_perturb = lax.dynamic_slice_in_dim(perturb, column * slice_width, slice_width, 1).astype(F32)
    new_perturb = (own_perturb + 0.5 * own_cols / jnp.sqrt(mean_square + 1e-06)).astype(BF16)

    return (new_perturb, weights[0], weights[1])


def solution(mesh):
    in_specs = (
        P("dom", None),
        P("dom", None),
        P(None, "feat"),
        P(None, "feat"),
        P("feat"),
        P("dom", "feat"),
        P("dom", None),
        P("dom", None, None),
        P("dom", None),
    )
    out_specs = (P("dom", "feat"), P(None, "feat"), P(None, "feat"))

    return jax.shard_map(per_device, mesh=mesh, in_specs=in_specs, out_specs=out_specs, check_vma=False)
```

```python
import jax
import jax.numpy as jnp
from jax import lax
from jax.sharding import PartitionSpec as P


K = 15
NOFF = 4
F32 = jnp.float32
BF16 = jnp.bfloat16
HIGH = lax.Precision.HIGHEST


def from_behind(x, axis, by):
    size = lax.axis_size(axis)
    return lax.ppermute(x, axis, [(i, (i + by) % size) for i in range(size)])


def offset_of(direction):
    return direction - 2 if direction < 2 else direction - 1


def contract_rows(left, right, precision=None):
    return lax.dot_general(
        left, right, (((0,), (0,)), ((), ())), preferred_element_type=F32, precision=precision
    )


def gather_all(x, axis):
    n = lax.axis_size(axis)
    rep = jnp.broadcast_to(x[None], (n,) + x.shape).reshape((n * x.shape[0],) + x.shape[1:])
    out = lax.all_to_all(rep, axis, 0, 0, tiled=True)
    return out.reshape((n,) + x.shape)


def per_device(features, perturb, w_self, w_neigh, bias, upstream, hub_rows, send_rows, neighbors):
    rows_here, feat_in = features.shape
    hidden_here = w_self.shape[1]
    slots = send_rows.shape[2]
    hub_dev = hub_rows.shape[1]
    dom_count = lax.axis_size("dom")
    feat_count = lax.axis_size("feat")
    column = lax.axis_index("feat")
    slice_width = feat_in // feat_count
    halo_rows = NOFF * slots
    table_rows = rows_here + halo_rows + dom_count * hub_dev

    perturbed = (features.astype(F32) + perturb.astype(F32)).astype(BF16)

    send_flat = send_rows[0].reshape(halo_rows)
    pick = (send_flat[:, None] == lax.broadcasted_iota(jnp.int32, (halo_rows, rows_here), 1))
    hub_pick = (hub_rows[0][:, None] == lax.broadcasted_iota(jnp.int32, (hub_dev, rows_here), 1))
    halo_out = jnp.dot(pick.astype(BF16), perturbed, preferred_element_type=F32).astype(BF16)
    hub_out = jnp.dot(hub_pick.astype(BF16), perturbed, preferred_element_type=F32).astype(BF16)

    pieces = [
        from_behind(halo_out[o * slots : (o + 1) * slots], "dom", offset_of(o))
        for o in range(NOFF)
    ]
    hubs = gather_all(hub_out, "dom").reshape(dom_count * hub_dev, feat_in)
    table = jnp.concatenate([perturbed] + pieces + [hubs], 0)

    t_iota = lax.broadcasted_iota(jnp.int32, (rows_here, K, table_rows), 2)
    counts = jnp.sum((neighbors[:, :, None] == t_iota).astype(F32), axis=1)
    gathered_sum = jnp.dot(counts.astype(BF16), table, preferred_element_type=F32)
    neighbor_mean = (gathered_sum / K).astype(BF16)

    preact = jnp.dot(perturbed, w_self, preferred_element_type=F32)
    preact = preact + jnp.dot(neighbor_mean, w_neigh, preferred_element_type=F32) + bias
    sigmoid_pre = jax.nn.sigmoid(preact)
    grad_pre = (
        upstream.astype(F32) * sigmoid_pre * (1.0 + preact * (1.0 - sigmoid_pre))
    ).astype(BF16)

    payload = jnp.concatenate([grad_pre, w_self, w_neigh], 0)
    got = jnp.stack(
        [payload] + [from_behind(payload, "feat", shift) for shift in range(1, feat_count)]
    )

    part_self = contract_rows(perturbed, grad_pre)
    part_neigh = contract_rows(neighbor_mean, grad_pre)
    weight_flat = jnp.concatenate([part_self.reshape(-1), part_neigh.reshape(-1)])
    weight_recv = lax.all_to_all(weight_flat.reshape(dom_count, -1, 128), "dom", 0, 0, tiled=True)

    gp_all = got[:, :rows_here]
    ws_all = got[:, rows_here : rows_here + feat_in]
    wn_all = got[:, rows_here + feat_in :]
    dims = (((0, 2), (0, 2)), ((), ()))
    own_grad = lax.dot_general(gp_all, ws_all, dims, preferred_element_type=F32)
    spread = lax.dot_general(gp_all, wn_all, dims, preferred_element_type=F32) / K

    table_grad = contract_rows(counts, spread, HIGH)

    returned = jnp.concatenate(
        [
            from_behind(
                table_grad[rows_here + o * slots : rows_here + (o + 1) * slots],
                "dom",
                -offset_of(o),
            )
            for o in range(NOFF)
        ],
        0,
    )

    weight_part = jnp.sum(weight_recv.reshape(dom_count, -1, 128), axis=0)
    hub_chunks = table_grad[rows_here + halo_rows :].reshape(dom_count, hub_dev, feat_in)
    weight_rep = jnp.broadcast_to(weight_part[None], (dom_count,) + weight_part.shape)
    sent = jnp.concatenate([hub_chunks, weight_rep], 1)
    recv = lax.all_to_all(sent, "dom", 0, 0, tiled=True).reshape(dom_count, -1)
    hub_total = jnp.sum(recv[:, : hub_dev * feat_in], axis=0).reshape(hub_dev, feat_in)
    weights = recv[:, hub_dev * feat_in :].reshape(2, feat_in, hidden_here)

    grad_in = own_grad + table_grad[:rows_here]
    grad_in = grad_in + contract_rows(pick.astype(F32), returned, HIGH)
    grad_in = grad_in + contract_rows(hub_pick.astype(F32), hub_total, HIGH)

    mean_square = jnp.mean(grad_in * grad_in, axis=1, keepdims=True)
    own_cols = lax.dynamic_slice_in_dim(grad_in, column * slice_width, slice_width, 1)
    own_perturb = lax.dynamic_slice_in_dim(perturb, column * slice_width, slice_width, 1).astype(F32)
    new_perturb = (own_perturb + 0.5 * own_cols / jnp.sqrt(mean_square + 1e-06)).astype(BF16)

    return (new_perturb, weights[0], weights[1])


def solution(mesh):
    in_specs = (
        P("dom", None),
        P("dom", None),
        P(None, "feat"),
        P(None, "feat"),
        P("feat"),
        P("dom", "feat"),
        P("dom", None),
        P("dom", None, None),
        P("dom", None),
    )
    out_specs = (P("dom", "feat"), P(None, "feat"), P(None, "feat"))

    return jax.shard_map(per_device, mesh=mesh, in_specs=in_specs, out_specs=out_specs, check_vma=False)
```

```python
import jax
import jax.numpy as jnp
from jax import lax
from jax.sharding import PartitionSpec as P


K = 15
NOFF = 4
F32 = jnp.float32
BF16 = jnp.bfloat16
HIGH = lax.Precision.HIGHEST


def from_behind(x, axis, by):
    size = lax.axis_size(axis)
    return lax.ppermute(x, axis, [(i, (i + by) % size) for i in range(size)])


def offset_of(direction):
    return direction - 2 if direction < 2 else direction - 1


def contract_rows(left, right, precision=None):
    return lax.dot_general(
        left, right, (((0,), (0,)), ((), ())), preferred_element_type=F32, precision=precision
    )


def gather_all(x, axis):
    n = lax.axis_size(axis)
    rep = jnp.broadcast_to(x[None], (n,) + x.shape).reshape((n * x.shape[0],) + x.shape[1:])
    out = lax.all_to_all(rep, axis, 0, 0, tiled=True)
    return out.reshape((n,) + x.shape)


def per_device(features, perturb, w_self, w_neigh, bias, upstream, hub_rows, send_rows, neighbors):
    rows_here, feat_in = features.shape
    hidden_here = w_self.shape[1]
    slots = send_rows.shape[2]
    hub_dev = hub_rows.shape[1]
    dom_count = lax.axis_size("dom")
    feat_count = lax.axis_size("feat")
    column = lax.axis_index("feat")
    slice_width = feat_in // feat_count
    halo_rows = NOFF * slots
    table_rows = rows_here + halo_rows + dom_count * hub_dev

    perturbed = (features.astype(F32) + perturb.astype(F32)).astype(BF16)

    send_flat = send_rows[0].reshape(halo_rows)
    pick = (send_flat[:, None] == lax.broadcasted_iota(jnp.int32, (halo_rows, rows_here), 1))
    hub_pick = (hub_rows[0][:, None] == lax.broadcasted_iota(jnp.int32, (hub_dev, rows_here), 1))
    halo_out = jnp.dot(pick.astype(BF16), perturbed, preferred_element_type=F32).astype(BF16)
    hub_out = jnp.dot(hub_pick.astype(BF16), perturbed, preferred_element_type=F32).astype(BF16)

    pieces = [
        from_behind(halo_out[o * slots : (o + 1) * slots], "dom", offset_of(o))
        for o in range(NOFF)
    ]
    pad_rows = 8 - hub_dev % 8 if hub_dev % 8 else 0
    hub_tile = jnp.pad(hub_out, ((0, pad_rows), (0, 0)))
    hubs = gather_all(hub_tile, "dom")[:, :hub_dev].reshape(dom_count * hub_dev, feat_in)
    table = jnp.concatenate([perturbed] + pieces + [hubs], 0)

    t_iota = lax.broadcasted_iota(jnp.int32, (rows_here, K, table_rows), 2)
    counts = jnp.sum((neighbors[:, :, None] == t_iota).astype(F32), axis=1)
    gathered_sum = jnp.dot(counts.astype(BF16), table, preferred_element_type=F32)
    neighbor_mean = (gathered_sum / K).astype(BF16)

    preact = jnp.dot(perturbed, w_self, preferred_element_type=F32)
    preact = preact + jnp.dot(neighbor_mean, w_neigh, preferred_element_type=F32) + bias
    sigmoid_pre = jax.nn.sigmoid(preact)
    grad_pre = (
        upstream.astype(F32) * sigmoid_pre * (1.0 + preact * (1.0 - sigmoid_pre))
    ).astype(BF16)

    payload = jnp.concatenate([grad_pre, w_self, w_neigh], 0)
    got = jnp.stack(
        [payload] + [from_behind(payload, "feat", shift) for shift in range(1, feat_count)]
    )

    part_self = contract_rows(perturbed, grad_pre)
    part_neigh = contract_rows(neighbor_mean, grad_pre)
    weight_flat = jnp.concatenate([part_self.reshape(-1), part_neigh.reshape(-1)])
    weight_recv = lax.all_to_all(weight_flat.reshape(dom_count, -1, 128), "dom", 0, 0, tiled=True)

    gp_all = got[:, :rows_here]
    ws_all = got[:, rows_here : rows_here + feat_in]
    wn_all = got[:, rows_here + feat_in :]
    dims = (((0, 2), (0, 2)), ((), ()))
    own_grad = lax.dot_general(gp_all, ws_all, dims, preferred_element_type=F32)
    spread = lax.dot_general(gp_all, wn_all, dims, preferred_element_type=F32) / K

    table_grad = contract_rows(counts, spread, HIGH)

    returned = jnp.concatenate(
        [
            from_behind(
                table_grad[rows_here + o * slots : rows_here + (o + 1) * slots],
                "dom",
                -offset_of(o),
            )
            for o in range(NOFF)
        ],
        0,
    )

    weight_part = jnp.sum(weight_recv.reshape(dom_count, -1, 128), axis=0)
    hub_chunks = table_grad[rows_here + halo_rows :].reshape(dom_count, hub_dev, feat_in)
    weight_rep = jnp.broadcast_to(weight_part[None], (dom_count,) + weight_part.shape)
    sent = jnp.concatenate([hub_chunks, weight_rep], 1)
    recv = lax.all_to_all(sent, "dom", 0, 0, tiled=True)
    hub_total = jnp.sum(recv[:, :hub_dev], axis=0)
    weights = recv[:, hub_dev:].reshape(2, feat_in, hidden_here)

    grad_in = own_grad + table_grad[:rows_here]
    grad_in = grad_in + contract_rows(pick.astype(F32), returned, HIGH)
    grad_in = grad_in + contract_rows(hub_pick.astype(F32), hub_total, HIGH)

    mean_square = jnp.mean(grad_in * grad_in, axis=1, keepdims=True)
    own_cols = lax.dynamic_slice_in_dim(grad_in, column * slice_width, slice_width, 1)
    own_perturb = lax.dynamic_slice_in_dim(perturb, column * slice_width, slice_width, 1).astype(F32)
    new_perturb = (own_perturb + 0.5 * own_cols / jnp.sqrt(mean_square + 1e-06)).astype(BF16)

    return (new_perturb, weights[0], weights[1])


def solution(mesh):
    in_specs = (
        P("dom", None),
        P("dom", None),
        P(None, "feat"),
        P(None, "feat"),
        P("feat"),
        P("dom", "feat"),
        P("dom", None),
        P("dom", None, None),
        P("dom", None),
    )
    out_specs = (P("dom", "feat"), P(None, "feat"), P(None, "feat"))

    return jax.shard_map(per_device, mesh=mesh, in_specs=in_specs, out_specs=out_specs, check_vma=False)
```

```python
import jax
import jax.numpy as jnp
from jax import lax
from jax.sharding import PartitionSpec as P


K = 15
NOFF = 4
F32 = jnp.float32
BF16 = jnp.bfloat16
HIGH = lax.Precision.HIGHEST


def from_behind(x, axis, by):
    size = lax.axis_size(axis)
    return lax.ppermute(x, axis, [(i, (i + by) % size) for i in range(size)])


def offset_of(direction):
    return direction - 2 if direction < 2 else direction - 1


def contract_rows(left, right, precision=None):
    return lax.dot_general(
        left, right, (((0,), (0,)), ((), ())), preferred_element_type=F32, precision=precision
    )


def gather_all(x, axis):
    n = lax.axis_size(axis)
    rep = jnp.broadcast_to(x[None], (n,) + x.shape).reshape((n * x.shape[0],) + x.shape[1:])
    out = lax.all_to_all(rep, axis, 0, 0, tiled=True)
    return out.reshape((n,) + x.shape)


def per_device(features, perturb, w_self, w_neigh, bias, upstream, hub_rows, send_rows, neighbors):
    rows_here, feat_in = features.shape
    hidden_here = w_self.shape[1]
    slots = send_rows.shape[2]
    hub_dev = hub_rows.shape[1]
    dom_count = lax.axis_size("dom")
    feat_count = lax.axis_size("feat")
    column = lax.axis_index("feat")
    slice_width = feat_in // feat_count
    halo_rows = NOFF * slots
    table_rows = rows_here + halo_rows + dom_count * hub_dev

    perturbed = (features.astype(F32) + perturb.astype(F32)).astype(BF16)

    send_flat = send_rows[0].reshape(halo_rows)
    pick = (send_flat[:, None] == lax.broadcasted_iota(jnp.int32, (halo_rows, rows_here), 1))
    hub_pick = (hub_rows[0][:, None] == lax.broadcasted_iota(jnp.int32, (hub_dev, rows_here), 1))
    halo_out = jnp.dot(pick.astype(BF16), perturbed, preferred_element_type=F32).astype(BF16)
    hub_out = jnp.dot(hub_pick.astype(BF16), perturbed, preferred_element_type=F32).astype(BF16)

    halo_pad = -slots % 16
    pieces = [
        from_behind(
            jnp.pad(halo_out[o * slots : (o + 1) * slots], ((0, halo_pad), (0, 0))),
            "dom",
            offset_of(o),
        )[:slots]
        for o in range(NOFF)
    ]
    pad_rows = 8 - hub_dev % 8 if hub_dev % 8 else 0
    hub_tile = jnp.pad(hub_out, ((0, pad_rows), (0, 0)))
    hubs = gather_all(hub_tile, "dom")[:, :hub_dev].reshape(dom_count * hub_dev, feat_in)
    table = jnp.concatenate([perturbed] + pieces + [hubs], 0)

    t_iota = lax.broadcasted_iota(jnp.int32, (rows_here, K, table_rows), 2)
    counts = jnp.sum((neighbors[:, :, None] == t_iota).astype(F32), axis=1)
    gathered_sum = jnp.dot(counts.astype(BF16), table, preferred_element_type=F32)
    neighbor_mean = (gathered_sum / K).astype(BF16)

    preact = jnp.dot(perturbed, w_self, preferred_element_type=F32)
    preact = preact + jnp.dot(neighbor_mean, w_neigh, preferred_element_type=F32) + bias
    sigmoid_pre = jax.nn.sigmoid(preact)
    grad_pre = (
        upstream.astype(F32) * sigmoid_pre * (1.0 + preact * (1.0 - sigmoid_pre))
    ).astype(BF16)

    payload = jnp.concatenate([grad_pre, w_self, w_neigh], 0)
    got = jnp.stack(
        [payload] + [from_behind(payload, "feat", shift) for shift in range(1, feat_count)]
    )

    part_self = contract_rows(perturbed, grad_pre)
    part_neigh = contract_rows(neighbor_mean, grad_pre)
    weight_flat = jnp.concatenate([part_self.reshape(-1), part_neigh.reshape(-1)])
    weight_recv = lax.all_to_all(weight_flat.reshape(dom_count, -1, 128), "dom", 0, 0, tiled=True)

    gp_all = got[:, :rows_here]
    ws_all = got[:, rows_here : rows_here + feat_in]
    wn_all = got[:, rows_here + feat_in :]
    dims = (((0, 2), (0, 2)), ((), ()))
    own_grad = lax.dot_general(gp_all, ws_all, dims, preferred_element_type=F32)
    spread = lax.dot_general(gp_all, wn_all, dims, preferred_element_type=F32) / K

    table_grad = contract_rows(counts, spread, HIGH)

    returned = jnp.concatenate(
        [
            from_behind(
                table_grad[rows_here + o * slots : rows_here + (o + 1) * slots],
                "dom",
                -offset_of(o),
            )
            for o in range(NOFF)
        ],
        0,
    )

    weight_part = jnp.sum(weight_recv.reshape(dom_count, -1, 128), axis=0)
    hub_chunks = table_grad[rows_here + halo_rows :].reshape(dom_count, hub_dev, feat_in)
    weight_rep = jnp.broadcast_to(weight_part[None], (dom_count,) + weight_part.shape)
    sent = jnp.concatenate([hub_chunks, weight_rep], 1)
    recv = lax.all_to_all(sent, "dom", 0, 0, tiled=True).reshape(dom_count, -1)
    hub_total = jnp.sum(recv[:, : hub_dev * feat_in], axis=0).reshape(hub_dev, feat_in)
    weights = recv[:, hub_dev * feat_in :].reshape(2, feat_in, hidden_here)

    grad_in = own_grad + table_grad[:rows_here]
    grad_in = grad_in + contract_rows(pick.astype(F32), returned, HIGH)
    grad_in = grad_in + contract_rows(hub_pick.astype(F32), hub_total, HIGH)

    mean_square = jnp.mean(grad_in * grad_in, axis=1, keepdims=True)
    own_cols = lax.dynamic_slice_in_dim(grad_in, column * slice_width, slice_width, 1)
    own_perturb = lax.dynamic_slice_in_dim(perturb, column * slice_width, slice_width, 1).astype(F32)
    new_perturb = (own_perturb + 0.5 * own_cols / jnp.sqrt(mean_square + 1e-06)).astype(BF16)

    return (new_perturb, weights[0], weights[1])


def solution(mesh):
    in_specs = (
        P("dom", None),
        P("dom", None),
        P(None, "feat"),
        P(None, "feat"),
        P("feat"),
        P("dom", "feat"),
        P("dom", None),
        P("dom", None, None),
        P("dom", None),
    )
    out_specs = (P("dom", "feat"), P(None, "feat"), P(None, "feat"))

    return jax.shard_map(per_device, mesh=mesh, in_specs=in_specs, out_specs=out_specs, check_vma=False)
```

```python
import jax
import jax.numpy as jnp
from jax import lax
from jax.sharding import PartitionSpec as P


K = 15
NOFF = 4
F32 = jnp.float32
BF16 = jnp.bfloat16
HIGH = lax.Precision.HIGHEST


def from_behind(x, axis, by):
    size = lax.axis_size(axis)
    return lax.ppermute(x, axis, [(i, (i + by) % size) for i in range(size)])


def offset_of(direction):
    return direction - 2 if direction < 2 else direction - 1


def contract_rows(left, right, precision=None):
    return lax.dot_general(
        left, right, (((0,), (0,)), ((), ())), preferred_element_type=F32, precision=precision
    )


def gather_all(x, axis):
    n = lax.axis_size(axis)
    rep = jnp.broadcast_to(x[None], (n,) + x.shape).reshape((n * x.shape[0],) + x.shape[1:])
    out = lax.all_to_all(rep, axis, 0, 0, tiled=True)
    return out.reshape((n,) + x.shape)


def per_device(features, perturb, w_self, w_neigh, bias, upstream, hub_rows, send_rows, neighbors):
    rows_here, feat_in = features.shape
    hidden_here = w_self.shape[1]
    slots = send_rows.shape[2]
    hub_dev = hub_rows.shape[1]
    dom_count = lax.axis_size("dom")
    feat_count = lax.axis_size("feat")
    column = lax.axis_index("feat")
    slice_width = feat_in // feat_count
    halo_rows = NOFF * slots
    table_rows = rows_here + halo_rows + dom_count * hub_dev

    perturbed = (features.astype(F32) + perturb.astype(F32)).astype(BF16)

    send_flat = send_rows[0].reshape(halo_rows)
    pick = (send_flat[:, None] == lax.broadcasted_iota(jnp.int32, (halo_rows, rows_here), 1))
    hub_pick = (hub_rows[0][:, None] == lax.broadcasted_iota(jnp.int32, (hub_dev, rows_here), 1))
    halo_out = jnp.dot(pick.astype(BF16), perturbed, preferred_element_type=F32).astype(BF16)
    hub_out = jnp.dot(hub_pick.astype(BF16), perturbed, preferred_element_type=F32).astype(BF16)

    t_iota = lax.broadcasted_iota(jnp.int32, (rows_here, K, table_rows), 2)
    counts = jnp.sum((neighbors[:, :, None] == t_iota).astype(F32), axis=1)
    halo_out, counts = lax.optimization_barrier((halo_out, counts))

    pieces = [
        from_behind(halo_out[o * slots : (o + 1) * slots], "dom", offset_of(o))
        for o in range(NOFF)
    ]
    pad_rows = 8 - hub_dev % 8 if hub_dev % 8 else 0
    hub_tile = jnp.pad(hub_out, ((0, pad_rows), (0, 0)))
    hubs = gather_all(hub_tile, "dom")[:, :hub_dev].reshape(dom_count * hub_dev, feat_in)
    table = jnp.concatenate([perturbed] + pieces + [hubs], 0)

    gathered_sum = jnp.dot(counts.astype(BF16), table, preferred_element_type=F32)
    neighbor_mean = (gathered_sum / K).astype(BF16)

    preact = jnp.dot(perturbed, w_self, preferred_element_type=F32)
    preact = preact + jnp.dot(neighbor_mean, w_neigh, preferred_element_type=F32) + bias
    sigmoid_pre = jax.nn.sigmoid(preact)
    grad_pre = (
        upstream.astype(F32) * sigmoid_pre * (1.0 + preact * (1.0 - sigmoid_pre))
    ).astype(BF16)

    payload = jnp.concatenate([grad_pre, w_self, w_neigh], 0)
    got = jnp.stack(
        [payload] + [from_behind(payload, "feat", shift) for shift in range(1, feat_count)]
    )

    part_self = contract_rows(perturbed, grad_pre)
    part_neigh = contract_rows(neighbor_mean, grad_pre)
    weight_flat = jnp.concatenate([part_self.reshape(-1), part_neigh.reshape(-1)])
    weight_recv = lax.all_to_all(weight_flat.reshape(dom_count, -1, 128), "dom", 0, 0, tiled=True)

    gp_all = got[:, :rows_here]
    ws_all = got[:, rows_here : rows_here + feat_in]
    wn_all = got[:, rows_here + feat_in :]
    dims = (((0, 2), (0, 2)), ((), ()))
    own_grad = lax.dot_general(gp_all, ws_all, dims, preferred_element_type=F32)
    spread = lax.dot_general(gp_all, wn_all, dims, preferred_element_type=F32) / K

    table_grad = contract_rows(counts, spread, HIGH)

    returned = jnp.concatenate(
        [
            from_behind(
                table_grad[rows_here + o * slots : rows_here + (o + 1) * slots],
                "dom",
                -offset_of(o),
            )
            for o in range(NOFF)
        ],
        0,
    )

    weight_part = jnp.sum(weight_recv.reshape(dom_count, -1, 128), axis=0)
    hub_chunks = table_grad[rows_here + halo_rows :].reshape(dom_count, hub_dev, feat_in)
    weight_rep = jnp.broadcast_to(weight_part[None], (dom_count,) + weight_part.shape)
    sent = jnp.concatenate([hub_chunks, weight_rep], 1)
    recv = lax.all_to_all(sent, "dom", 0, 0, tiled=True).reshape(dom_count, -1)
    hub_total = jnp.sum(recv[:, : hub_dev * feat_in], axis=0).reshape(hub_dev, feat_in)
    weights = recv[:, hub_dev * feat_in :].reshape(2, feat_in, hidden_here)

    grad_in = own_grad + table_grad[:rows_here]
    grad_in = grad_in + contract_rows(pick.astype(F32), returned, HIGH)
    grad_in = grad_in + contract_rows(hub_pick.astype(F32), hub_total, HIGH)

    mean_square = jnp.mean(grad_in * grad_in, axis=1, keepdims=True)
    own_cols = lax.dynamic_slice_in_dim(grad_in, column * slice_width, slice_width, 1)
    own_perturb = lax.dynamic_slice_in_dim(perturb, column * slice_width, slice_width, 1).astype(F32)
    new_perturb = (own_perturb + 0.5 * own_cols / jnp.sqrt(mean_square + 1e-06)).astype(BF16)

    return (new_perturb, weights[0], weights[1])


def solution(mesh):
    in_specs = (
        P("dom", None),
        P("dom", None),
        P(None, "feat"),
        P(None, "feat"),
        P("feat"),
        P("dom", "feat"),
        P("dom", None),
        P("dom", None, None),
        P("dom", None),
    )
    out_specs = (P("dom", "feat"), P(None, "feat"), P(None, "feat"))

    return jax.shard_map(per_device, mesh=mesh, in_specs=in_specs, out_specs=out_specs, check_vma=False)
```

```python
import jax
import jax.numpy as jnp
from jax import lax
from jax.sharding import PartitionSpec as P


K = 15
NOFF = 4
F32 = jnp.float32
BF16 = jnp.bfloat16
HIGH = lax.Precision.HIGHEST


def from_behind(x, axis, by):
    size = lax.axis_size(axis)
    return lax.ppermute(x, axis, [(i, (i + by) % size) for i in range(size)])


def offset_of(direction):
    return direction - 2 if direction < 2 else direction - 1


def contract_rows(left, right, precision=None):
    return lax.dot_general(
        left, right, (((0,), (0,)), ((), ())), preferred_element_type=F32, precision=precision
    )


def gather_all(x, axis):
    n = lax.axis_size(axis)
    rep = jnp.broadcast_to(x[None], (n,) + x.shape).reshape((n * x.shape[0],) + x.shape[1:])
    out = lax.all_to_all(rep, axis, 0, 0, tiled=True)
    return out.reshape((n,) + x.shape)


def per_device(features, perturb, w_self, w_neigh, bias, upstream, hub_rows, send_rows, neighbors):
    rows_here, feat_in = features.shape
    hidden_here = w_self.shape[1]
    slots = send_rows.shape[2]
    hub_dev = hub_rows.shape[1]
    dom_count = lax.axis_size("dom")
    feat_count = lax.axis_size("feat")
    column = lax.axis_index("feat")
    slice_width = feat_in // feat_count
    halo_rows = NOFF * slots
    table_rows = rows_here + halo_rows + dom_count * hub_dev

    perturbed = (features.astype(F32) + perturb.astype(F32)).astype(BF16)

    send_flat = send_rows[0].reshape(halo_rows)
    pick = (send_flat[:, None] == lax.broadcasted_iota(jnp.int32, (halo_rows, rows_here), 1))
    hub_pick = (hub_rows[0][:, None] == lax.broadcasted_iota(jnp.int32, (hub_dev, rows_here), 1))
    halo_out = jnp.dot(pick.astype(BF16), perturbed, preferred_element_type=F32).astype(BF16)
    hub_out = jnp.dot(hub_pick.astype(BF16), perturbed, preferred_element_type=F32).astype(BF16)

    pieces = [
        from_behind(halo_out[o * slots : (o + 1) * slots], "dom", offset_of(o))
        for o in range(NOFF)
    ]
    pad_rows = 8 - hub_dev % 8 if hub_dev % 8 else 0
    hub_tile = jnp.pad(hub_out, ((0, pad_rows), (0, 0)))
    hubs = gather_all(hub_tile, "dom")[:, :hub_dev].reshape(dom_count * hub_dev, feat_in)
    table = jnp.concatenate([perturbed] + pieces + [hubs], 0)

    t_iota = lax.broadcasted_iota(jnp.int32, (rows_here, K, table_rows), 2)
    counts = jnp.sum((neighbors[:, :, None] == t_iota).astype(F32), axis=1)
    gathered_sum = jnp.dot(counts.astype(BF16), table, preferred_element_type=F32)
    neighbor_mean = (gathered_sum / K).astype(BF16)

    preact = jnp.dot(perturbed, w_self, preferred_element_type=F32)
    preact = preact + jnp.dot(neighbor_mean, w_neigh, preferred_element_type=F32) + bias
    sigmoid_pre = jax.nn.sigmoid(preact)
    grad_pre = (
        upstream.astype(F32) * sigmoid_pre * (1.0 + preact * (1.0 - sigmoid_pre))
    ).astype(BF16)

    payload = jnp.concatenate([grad_pre, w_self, w_neigh], 0)
    got = jnp.stack(
        [payload] + [from_behind(payload, "feat", shift) for shift in range(1, feat_count)]
    )

    part_self = contract_rows(perturbed, grad_pre)
    part_neigh = contract_rows(neighbor_mean, grad_pre)
    weight_flat = jnp.concatenate([part_self.reshape(-1), part_neigh.reshape(-1)])
    weight_recv = lax.all_to_all(weight_flat.reshape(dom_count, -1, 128), "dom", 0, 0, tiled=True)

    gp_all = got[:, :rows_here]
    ws_all = got[:, rows_here : rows_here + feat_in]
    wn_all = got[:, rows_here + feat_in :]
    dims = (((0, 2), (0, 2)), ((), ()))
    own_grad = lax.dot_general(gp_all, ws_all, dims, preferred_element_type=F32)
    spread = lax.dot_general(gp_all, wn_all, dims, preferred_element_type=F32) / K

    table_grad = contract_rows(counts, spread, HIGH)

    returned = jnp.concatenate(
        [
            from_behind(
                table_grad[rows_here + o * slots : rows_here + (o + 1) * slots],
                "dom",
                -offset_of(o),
            )
            for o in range(NOFF)
        ],
        0,
    )

    weight_part = jnp.sum(weight_recv.reshape(dom_count, -1, 128), axis=0)
    hub_chunks = table_grad[rows_here + halo_rows :].reshape(dom_count, hub_dev, feat_in)
    weight_rep = jnp.broadcast_to(weight_part[None], (dom_count,) + weight_part.shape)
    sent = jnp.concatenate([hub_chunks, weight_rep], 1)
    recv3 = lax.all_to_all(sent, "dom", 0, 0, tiled=True)
    recv = recv3.reshape(dom_count, -1)
    hub_total = jnp.sum(recv[:, : hub_dev * feat_in], axis=0).reshape(hub_dev, feat_in)
    weights = recv3[:, hub_dev:].reshape(2, feat_in, hidden_here)

    grad_in = own_grad + table_grad[:rows_here]
    grad_in = grad_in + contract_rows(pick.astype(F32), returned, HIGH)
    grad_in = grad_in + contract_rows(hub_pick.astype(F32), hub_total, HIGH)

    mean_square = jnp.mean(grad_in * grad_in, axis=1, keepdims=True)
    own_cols = lax.dynamic_slice_in_dim(grad_in, column * slice_width, slice_width, 1)
    own_perturb = lax.dynamic_slice_in_dim(perturb, column * slice_width, slice_width, 1).astype(F32)
    new_perturb = (own_perturb + 0.5 * own_cols / jnp.sqrt(mean_square + 1e-06)).astype(BF16)

    return (new_perturb, weights[0], weights[1])


def solution(mesh):
    in_specs = (
        P("dom", None),
        P("dom", None),
        P(None, "feat"),
        P(None, "feat"),
        P("feat"),
        P("dom", "feat"),
        P("dom", None),
        P("dom", None, None),
        P("dom", None),
    )
    out_specs = (P("dom", "feat"), P(None, "feat"), P(None, "feat"))

    return jax.shard_map(per_device, mesh=mesh, in_specs=in_specs, out_specs=out_specs, check_vma=False)
```
